256 devices in a mesh: tm: 32 (over z, x_lo, core), space: 8 (over x_hi, y).
Axes of the slice: x: 4 (x_hi: 2, x_lo: 2; x = x_hi * 2 + x_lo), y: 4, z: 8, core: 2. Of those that a mesh axis runs over, the one named last changes fastest.
Arguments:
- forcing: float32 [128, 32, 128, 128], P('tm', 'space'), may hold values from -6 to 6
- conductivity: float32 [32, 128, 128], P('space'), may hold values from 0.5 to 2
- guess: float32 [32, 32, 128, 128], P('tm', 'space'), may hold values from -6 to 6
Outputs:
- solution: float32 [128, 32, 128, 128], P('tm', 'space')
The draws below stay inside these ranges and needn't reach their ends.
All inputs are finite; a program needn't handle non-finite values.
Results may differ from the reference program's by a relative error of at most 0.00002.
Values sent between devices are 32-bit elements; how exact they have to be, the bound alone decides.
No kernel may reach another device: no remote copies, remote signals or barrier semaphores. Data moves between devices by JAX's collectives and lax.ppermute only.
A program may use at most 64 MiB of HBM per device.

```python
import math
import jax
import jax.numpy as jnp

SX = 128
SY = 128
CF = 4
NT = 128
NZ = 32
NC = 32
N_TM = 32


def levels(stream_key, dims, split, low, largest):
    def one(position, blocks):
        steps = jax.random.uniform(jax.random.fold_in(jax.random.fold_in(stream_key, 6), position), (blocks,), jnp.float32, low / len(split), largest / len(split))
        return jnp.repeat(jnp.exp(steps), dims[position] // blocks).reshape((-1,) + (1,) * (len(dims) - position - 1))

    gain = one(*split[0])
    for cut in split[1:]:
        gain = gain * one(*cut)
    return gain


def gaussian(key, extent, spread, reach, shards=(), kind=jnp.bfloat16):
    entries = jax.random.normal(key, extent, jnp.float32) * spread
    if len(shards) > 0:
        entries = levels(key, extent, shards, -0.22, 0.18) * entries
    return jnp.clip(entries, min=-reach, max=reach).astype(kind)


def setup_inputs(seed: int = 0) -> dict:
    streams_of = jax.random.split(jax.random.key(seed), 4)
    forcing = gaussian(streams_of[0], (NT, NZ, SX, SY), 1.0, 6.0, ((0, 32), (1, 8)), jnp.float32)
    conductivity = jnp.clip(jnp.exp(math.log(2.0) - 1.3862944 * jax.random.uniform(streams_of[1], (NZ, SX, SY), jnp.float32) ** levels(streams_of[1], (NZ, SX, SY), ((0, 8),), -0.2, 0.2)), 0.5, 2.0)
    guess = gaussian(streams_of[2], (NC, NZ, SX, SY), 1.0, 6.0, ((0, 32), (1, 8)), jnp.float32)
    return dict(forcing=forcing, conductivity=conductivity, guess=guess)


step_length = 0.1


def neighbours(field):
    padded = jnp.pad(field, ((0, 0), (1, 1), (0, 0), (0, 0)))
    total = padded[:, :-2] + padded[:, 2:]
    total = total + jnp.roll(field, 1, axis=2) + jnp.roll(field, -1, axis=2)
    return total + jnp.roll(field, 1, axis=3) + jnp.roll(field, -1, axis=3)


def two_sweeps(start, target, weight, scaled):
    first = (target + weight * neighbours(start)) / scaled
    return (target + weight * neighbours(first)) / scaled


def reference(forcing, conductivity, guess):
    kappa = conductivity[None]
    fine_weight = step_length * kappa
    fine_scaled = 1.0 + 6.0 * fine_weight
    coarse_weight = CF * step_length * kappa
    coarse_scaled = 1.0 + 6.0 * coarse_weight
    sources = forcing.reshape(N_TM, CF, NZ, SX, SY)

    def fine_step(state, source):
        return two_sweeps(state, state + step_length * source, fine_weight, fine_scaled)

    def relax(anchor):
        states = [anchor]
        for index in range(1, CF):
            states.append(fine_step(states[-1], sources[:, index]))
        return jnp.stack(states, axis=1)

    anchor = guess
    states = relax(anchor)
    before = jnp.roll(states[:, CF - 1], 1, axis=0)
    defect = fine_step(before, sources[:, 0]) - anchor
    total = defect
    for turn in range(N_TM - 1):
        moved = jnp.roll(total, 1, axis=0)
        total = defect + two_sweeps(moved, moved, coarse_weight, coarse_scaled)
    anchor = anchor + total
    return relax(anchor).reshape(NT, NZ, SX, SY)
```

```python
import jax
import jax.numpy as jnp
from jax import lax
from jax.sharding import PartitionSpec as P

CF = 4


step_length = 0.1


def extended(block, sides, width):
    for axis, dim in sides:
        count = lax.axis_size(axis)
        forward = [(i, i + 1) for i in range(count - 1)]
        backward = [(target, source) for source, target in forward]
        low = lax.ppermute(
            lax.slice_in_dim(block, block.shape[dim] - width, None, axis=dim), axis, forward
        )
        high = lax.ppermute(lax.slice_in_dim(block, 0, width, axis=dim), axis, backward)
        block = jnp.concatenate([low, block, high], axis=dim)
    return block


def shifted(value, axis, steps):
    count = lax.axis_size(axis)
    pairs = [(source, (source + steps) % count) for source in range(count)]
    return lax.ppermute(value, axis, pairs)


def neighbours(field):
    middle = field[1:-1]
    total = field[:-2] + field[2:]
    total = total + jnp.roll(middle, 1, axis=1) + jnp.roll(middle, -1, axis=1)
    return total + jnp.roll(middle, 1, axis=2) + jnp.roll(middle, -1, axis=2)


def neighbours_closed(field):
    zero = jnp.zeros_like(field[:1])
    return neighbours(jnp.concatenate([zero, field, zero], axis=0))


def sweep_once(field, target, weight, scaled):
    return (target + weight * neighbours(field)) / scaled


def per_device(forcing, conductivity, guess):
    stacked = jnp.concatenate([conductivity[None], forcing], axis=0)
    widened = extended(stacked, (("space", 1),), 1)
    kappa_wide = widened[0]
    fine_weight = step_length * kappa_wide
    fine_scaled = 1.0 + 6.0 * fine_weight

    kappa_full = lax.all_gather(conductivity, "space", axis=0, tiled=True)
    coarse_weight = CF * step_length * kappa_full
    coarse_scaled = 1.0 + 6.0 * coarse_weight

    def advance(state, weight, scaled, source):
        padded = extended(state, (("space", 0),), 2)
        target = padded[1:-1]
        if source is not None:
            target = target + step_length * source
        first = sweep_once(padded, target, weight, scaled)
        return sweep_once(first, target[1:-1], weight[1:-1], scaled[1:-1])

    def fine_step(state, index):
        return advance(state, fine_weight, fine_scaled, widened[1 + index])

    def coarse_full(field):
        first = (field + coarse_weight * neighbours_closed(field)) / coarse_scaled
        return (field + coarse_weight * neighbours_closed(first)) / coarse_scaled

    def relax(anchor):
        states = [anchor]
        for index in range(1, CF):
            states.append(fine_step(states[-1], index))
        return states

    anchor = guess[0]
    states = relax(anchor)
    before = shifted(states[-1], "tm", 1)
    defect = fine_step(before, 0) - anchor

    count = lax.axis_size("tm")
    me = lax.axis_index("tm")
    depth = defect.shape[0]
    offset = lax.axis_index("space") * depth
    defect_full = lax.all_gather(defect, "space", axis=0, tiled=True)

    blocks = jnp.zeros((count,) + defect.shape, defect.dtype)
    blocks = lax.dynamic_update_index_in_dim(blocks, defect, me, 0)

    def chain(power, carried):
        field, blocks = carried
        field = coarse_full(field)
        piece = lax.dynamic_slice_in_dim(field, offset, depth, axis=0)
        blocks = lax.dynamic_update_index_in_dim(blocks, piece, (me + power) % count, 0)
        return field, blocks

    _, blocks = lax.fori_loop(1, count, chain, (defect_full, blocks))
    total = lax.psum_scatter(blocks, "tm", scatter_dimension=0, tiled=True)[0]
    anchor = anchor + total
    return jnp.stack(relax(anchor), axis=0)


def solution(mesh):
    in_specs = (P("tm", "space", None, None), P("space", None, None), P("tm", "space", None, None))
    out_specs = P("tm", "space", None, None)
    return jax.shard_map(
        per_device, mesh=mesh, in_specs=in_specs, out_specs=out_specs, check_vma=False
    )
```

```python
import functools

import jax
import jax.numpy as jnp
from jax import lax
from jax.experimental import pallas as pl
from jax.experimental.pallas import tpu as pltpu
from jax.sharding import PartitionSpec as P

CF = 4


step_length = 0.1


def extended(block, sides, width):
    for axis, dim in sides:
        count = lax.axis_size(axis)
        forward = [(i, i + 1) for i in range(count - 1)]
        backward = [(target, source) for source, target in forward]
        low = lax.ppermute(
            lax.slice_in_dim(block, block.shape[dim] - width, None, axis=dim), axis, forward
        )
        high = lax.ppermute(lax.slice_in_dim(block, 0, width, axis=dim), axis, backward)
        block = jnp.concatenate([low, block, high], axis=dim)
    return block


def shifted(value, axis, steps):
    count = lax.axis_size(axis)
    pairs = [(source, (source + steps) % count) for source in range(count)]
    return lax.ppermute(value, axis, pairs)


def neighbours(field):
    middle = field[1:-1]
    total = field[:-2] + field[2:]
    total = total + jnp.roll(middle, 1, axis=1) + jnp.roll(middle, -1, axis=1)
    return total + jnp.roll(middle, 1, axis=2) + jnp.roll(middle, -1, axis=2)


def sweep_once(field, target, weight, scaled):
    return (target + weight * neighbours(field)) / scaled


def column_slabs(slab, lag):
    n_tm = lax.axis_size("tm")
    n_sp = lax.axis_size("space")
    slots = []
    for t in range(n_sp):
        if t == 0 and lag == 0:
            slots.append(slab)
            continue
        pairs = []
        for k in range(n_tm):
            for q in range(n_sp):
                pairs.append((k * n_sp + q, ((k + lag) % n_tm) * n_sp + (q + t) % n_sp))
        slots.append(lax.ppermute(slab, ("tm", "space"), pairs))
    return jnp.stack(slots, axis=0)


def coarse_kernel(place_ref, slots_ref, w_ref, s_ref, o_ref, a_buf, b_buf):
    n_sp, depth, rows, cols = slots_ref.shape
    planes = n_sp * depth
    me = place_ref[0]
    power = place_ref[1]
    zero = jnp.zeros((rows, cols), jnp.float32)
    a_buf[0] = zero
    a_buf[planes + 1] = zero
    b_buf[0] = zero
    b_buf[planes + 1] = zero

    def load(q, carry):
        slot = lax.rem(me - q + n_sp, n_sp)
        for p in range(depth):
            a_buf[1 + q * depth + p] = slots_ref[slot, p]
        return carry

    lax.fori_loop(0, n_sp, load, 0)

    def sweep(src, dst, z):
        centre = src[z + 1]
        total = src[z] + src[z + 2]
        total = total + pltpu.roll(centre, 1, 0) + pltpu.roll(centre, rows - 1, 0)
        total = total + pltpu.roll(centre, 1, 1) + pltpu.roll(centre, cols - 1, 1)
        dst[z + 1] = (a_buf[z + 1] + w_ref[z] * total) / s_ref[z]

    def first(z, carry):
        sweep(a_buf, b_buf, z)
        return carry

    def second(z, carry):
        sweep(b_buf, a_buf, z)
        return carry

    def one(i, carry):
        lax.fori_loop(0, planes, first, 0)
        lax.fori_loop(0, planes, second, 0)
        return carry

    lax.fori_loop(0, power, one, 0)
    for p in range(depth):
        o_ref[p] = a_buf[1 + me * depth + p]


def coarse_power(power, place, slots, weight, scaled):
    n_sp, depth, rows, cols = slots.shape
    planes = n_sp * depth
    vmem = pltpu.MemorySpace.VMEM if hasattr(pltpu, "MemorySpace") else pltpu.VMEM
    return pl.pallas_call(
        coarse_kernel,
        out_shape=jax.ShapeDtypeStruct((depth, rows, cols), jnp.float32),
        in_specs=[
            pl.BlockSpec(memory_space=pltpu.SMEM),
            pl.BlockSpec(memory_space=vmem),
            pl.BlockSpec(memory_space=vmem),
            pl.BlockSpec(memory_space=vmem),
        ],
        out_specs=pl.BlockSpec(memory_space=vmem),
        scratch_shapes=[
            pltpu.VMEM((planes + 2, rows, cols), jnp.float32),
            pltpu.VMEM((planes + 2, rows, cols), jnp.float32),
        ],
        compiler_params=pltpu.CompilerParams(vmem_limit_bytes=48 * 1024 * 1024),
        cost_estimate=pl.CostEstimate(
            flops=2 * power * planes * rows * cols * 12,
            bytes_accessed=4 * planes * rows * cols * 3,
            transcendentals=0,
        ),
    )(jnp.stack([place, jnp.int32(power)]), slots, weight, scaled)


def per_device(forcing, conductivity, guess):
    stacked = jnp.concatenate([conductivity[None], forcing], axis=0)
    widened = extended(stacked, (("space", 1),), 1)
    kappa_wide = widened[0]
    fine_weight = step_length * kappa_wide
    fine_scaled = 1.0 + 6.0 * fine_weight

    n_sp = lax.axis_size("space")
    me_sp = lax.axis_index("space")
    order = lax.rem(me_sp - jnp.arange(n_sp, dtype=jnp.int32) + n_sp, n_sp)
    kappa_full = jnp.take(column_slabs(conductivity, 0), order, axis=0)
    kappa_full = kappa_full.reshape((-1,) + conductivity.shape[1:])
    coarse_weight = CF * step_length * kappa_full
    coarse_scaled = 1.0 + 6.0 * coarse_weight
    place = me_sp.astype(jnp.int32)

    def advance(state, weight, scaled, source):
        padded = extended(state, (("space", 0),), 2)
        target = padded[1:-1]
        if source is not None:
            target = target + step_length * source
        first = sweep_once(padded, target, weight, scaled)
        return sweep_once(first, target[1:-1], weight[1:-1], scaled[1:-1])

    def fine_step(state, index):
        return advance(state, fine_weight, fine_scaled, widened[1 + index])

    def relax(anchor):
        states = [anchor]
        for index in range(1, CF):
            states.append(fine_step(states[-1], index))
        return states

    anchor = guess[0]
    states = relax(anchor)
    before = shifted(states[-1], "tm", 1)
    defect = fine_step(before, 0) - anchor

    count = lax.axis_size("tm")
    total = defect
    lag = 1
    while lag < count:
        slots = column_slabs(total, lag)
        total = total + coarse_power(lag, place, slots, coarse_weight, coarse_scaled)
        lag *= 2
    anchor = anchor + total
    return jnp.stack(relax(anchor), axis=0)


def solution(mesh):
    in_specs = (P("tm", "space", None, None), P("space", None, None), P("tm", "space", None, None))
    out_specs = P("tm", "space", None, None)
    return jax.shard_map(
        per_device, mesh=mesh, in_specs=in_specs, out_specs=out_specs, check_vma=False
    )
```

```python
import functools

import jax
import jax.numpy as jnp
from jax import lax
from jax.experimental import pallas as pl
from jax.experimental.pallas import tpu as pltpu
from jax.sharding import PartitionSpec as P

CF = 4


step_length = 0.1


def extended(block, sides, width):
    for axis, dim in sides:
        count = lax.axis_size(axis)
        forward = [(i, i + 1) for i in range(count - 1)]
        backward = [(target, source) for source, target in forward]
        low = lax.ppermute(
            lax.slice_in_dim(block, block.shape[dim] - width, None, axis=dim), axis, forward
        )
        high = lax.ppermute(lax.slice_in_dim(block, 0, width, axis=dim), axis, backward)
        block = jnp.concatenate([low, block, high], axis=dim)
    return block


def shifted(value, axis, steps):
    count = lax.axis_size(axis)
    pairs = [(source, (source + steps) % count) for source in range(count)]
    return lax.ppermute(value, axis, pairs)


def neighbours(field):
    middle = field[1:-1]
    total = field[:-2] + field[2:]
    total = total + jnp.roll(middle, 1, axis=1) + jnp.roll(middle, -1, axis=1)
    return total + jnp.roll(middle, 1, axis=2) + jnp.roll(middle, -1, axis=2)


def sweep_once(field, target, weight, scaled):
    return (target + weight * neighbours(field)) / scaled


def column_slabs(slab, lag):
    if lag:
        slab = shifted(slab, "tm", lag)
    slots = [slab]
    for t in range(1, lax.axis_size("space")):
        slots.append(shifted(slab, "space", t))
    return jnp.stack(slots, axis=0)


def coarse_kernel(place_ref, slots_ref, w_ref, s_ref, o_ref, a_buf, b_buf):
    n_sp, depth, rows, cols = slots_ref.shape
    planes = n_sp * depth
    me = place_ref[0]
    power = place_ref[1]
    zero = jnp.zeros((rows, cols), jnp.float32)
    a_buf[0] = zero
    a_buf[planes + 1] = zero
    b_buf[0] = zero
    b_buf[planes + 1] = zero

    def load(q, carry):
        slot = lax.rem(me - q + n_sp, n_sp)
        for p in range(depth):
            a_buf[1 + q * depth + p] = slots_ref[slot, p]
        return carry

    lax.fori_loop(0, n_sp, load, 0)

    def sweep(src, dst, z):
        centre = src[z + 1]
        total = src[z] + src[z + 2]
        total = total + pltpu.roll(centre, 1, 0) + pltpu.roll(centre, rows - 1, 0)
        total = total + pltpu.roll(centre, 1, 1) + pltpu.roll(centre, cols - 1, 1)
        dst[z + 1] = (a_buf[z + 1] + w_ref[z] * total) / s_ref[z]

    def first(z, carry):
        sweep(a_buf, b_buf, z)
        return carry

    def second(z, carry):
        sweep(b_buf, a_buf, z)
        return carry

    def one(i, carry):
        lax.fori_loop(0, planes, first, 0, unroll=True)
        lax.fori_loop(0, planes, second, 0, unroll=True)
        return carry

    lax.fori_loop(0, power, one, 0)
    for p in range(depth):
        o_ref[p] = a_buf[1 + me * depth + p]


def coarse_power(power, place, slots, weight, scaled):
    n_sp, depth, rows, cols = slots.shape
    planes = n_sp * depth
    vmem = pltpu.MemorySpace.VMEM if hasattr(pltpu, "MemorySpace") else pltpu.VMEM
    return pl.pallas_call(
        coarse_kernel,
        out_shape=jax.ShapeDtypeStruct((depth, rows, cols), jnp.float32),
        in_specs=[
            pl.BlockSpec(memory_space=pltpu.SMEM),
            pl.BlockSpec(memory_space=vmem),
            pl.BlockSpec(memory_space=vmem),
            pl.BlockSpec(memory_space=vmem),
        ],
        out_specs=pl.BlockSpec(memory_space=vmem),
        scratch_shapes=[
            pltpu.VMEM((planes + 2, rows, cols), jnp.float32),
            pltpu.VMEM((planes + 2, rows, cols), jnp.float32),
        ],
        compiler_params=pltpu.CompilerParams(vmem_limit_bytes=48 * 1024 * 1024),
        cost_estimate=pl.CostEstimate(
            flops=2 * power * planes * rows * cols * 12,
            bytes_accessed=4 * planes * rows * cols * 3,
            transcendentals=0,
        ),
    )(jnp.stack([place, jnp.int32(power)]), slots, weight, scaled)


def per_device(forcing, conductivity, guess):
    stacked = jnp.concatenate([conductivity[None], forcing], axis=0)
    widened = extended(stacked, (("space", 1),), 1)
    kappa_wide = widened[0]
    fine_weight = step_length * kappa_wide
    fine_scaled = 1.0 + 6.0 * fine_weight

    n_sp = lax.axis_size("space")
    me_sp = lax.axis_index("space")
    order = lax.rem(me_sp - jnp.arange(n_sp, dtype=jnp.int32) + n_sp, n_sp)
    kappa_full = jnp.take(column_slabs(conductivity, 0), order, axis=0)
    kappa_full = kappa_full.reshape((-1,) + conductivity.shape[1:])
    coarse_weight = CF * step_length * kappa_full
    coarse_scaled = 1.0 + 6.0 * coarse_weight
    place = me_sp.astype(jnp.int32)

    def advance(state, weight, scaled, source):
        padded = extended(state, (("space", 0),), 2)
        target = padded[1:-1]
        if source is not None:
            target = target + step_length * source
        first = sweep_once(padded, target, weight, scaled)
        return sweep_once(first, target[1:-1], weight[1:-1], scaled[1:-1])

    def fine_step(state, index):
        return advance(state, fine_weight, fine_scaled, widened[1 + index])

    def relax(anchor):
        states = [anchor]
        for index in range(1, CF):
            states.append(fine_step(states[-1], index))
        return states

    anchor = guess[0]
    states = relax(anchor)
    before = shifted(states[-1], "tm", 1)
    defect = fine_step(before, 0) - anchor

    count = lax.axis_size("tm")
    total = defect
    lag = 1
    while lag < count:
        slots = column_slabs(total, lag)
        total = total + coarse_power(lag, place, slots, coarse_weight, coarse_scaled)
        lag *= 2
    anchor = anchor + total
    return jnp.stack(relax(anchor), axis=0)


def solution(mesh):
    in_specs = (P("tm", "space", None, None), P("space", None, None), P("tm", "space", None, None))
    out_specs = P("tm", "space", None, None)
    return jax.shard_map(
        per_device, mesh=mesh, in_specs=in_specs, out_specs=out_specs, check_vma=False
    )
```

```python
import functools

import jax
import jax.numpy as jnp
from jax import lax
from jax.experimental import pallas as pl
from jax.experimental.pallas import tpu as pltpu
from jax.sharding import PartitionSpec as P

CF = 4


step_length = 0.1


def extended(block, sides, width):
    for axis, dim in sides:
        count = lax.axis_size(axis)
        forward = [(i, i + 1) for i in range(count - 1)]
        backward = [(target, source) for source, target in forward]
        low = lax.ppermute(
            lax.slice_in_dim(block, block.shape[dim] - width, None, axis=dim), axis, forward
        )
        high = lax.ppermute(lax.slice_in_dim(block, 0, width, axis=dim), axis, backward)
        block = jnp.concatenate([low, block, high], axis=dim)
    return block


def shifted(value, axis, steps):
    count = lax.axis_size(axis)
    pairs = [(source, (source + steps) % count) for source in range(count)]
    return lax.ppermute(value, axis, pairs)


def neighbours(field):
    middle = field[1:-1]
    total = field[:-2] + field[2:]
    total = total + jnp.roll(middle, 1, axis=1) + jnp.roll(middle, -1, axis=1)
    return total + jnp.roll(middle, 1, axis=2) + jnp.roll(middle, -1, axis=2)


def sweep_once(field, target, weight, scaled):
    return (target + weight * neighbours(field)) / scaled


def column_slabs(slab, lag):
    if lag:
        slab = shifted(slab, "tm", lag)
    slots = [slab]
    for t in range(1, lax.axis_size("space")):
        slots.append(shifted(slab, "space", t))
    return jnp.stack(slots, axis=0)


def coarse_kernel(place_ref, slots_ref, w_ref, s_ref, o_ref, a_buf, b_buf):
    n_sp, depth, rows, cols = slots_ref.shape
    planes = n_sp * depth
    me = place_ref[0]
    power = place_ref[1]
    zero = jnp.zeros((rows, cols), jnp.float32)
    a_buf[0] = zero
    a_buf[planes + 1] = zero
    b_buf[0] = zero
    b_buf[planes + 1] = zero

    def load(q, carry):
        slot = lax.rem(me - q + n_sp, n_sp)
        for p in range(depth):
            a_buf[1 + q * depth + p] = slots_ref[slot, p]
        return carry

    lax.fori_loop(0, n_sp, load, 0)

    def sweep(src, dst, z):
        centre = src[z + 1]
        total = src[z] + src[z + 2]
        total = total + pltpu.roll(centre, 1, 0) + pltpu.roll(centre, rows - 1, 0)
        total = total + pltpu.roll(centre, 1, 1) + pltpu.roll(centre, cols - 1, 1)
        dst[z + 1] = (a_buf[z + 1] + w_ref[z] * total) / s_ref[z]

    def first(z, carry):
        sweep(a_buf, b_buf, z)
        return carry

    def second(z, carry):
        sweep(b_buf, a_buf, z)
        return carry

    def one(i, carry):
        lax.fori_loop(0, planes, first, 0, unroll=True)
        lax.fori_loop(0, planes, second, 0, unroll=True)
        return carry

    lax.fori_loop(0, power, one, 0)
    for p in range(depth):
        o_ref[p] = a_buf[1 + me * depth + p]


def coarse_power(power, place, slots, weight, scaled):
    n_sp, depth, rows, cols = slots.shape
    planes = n_sp * depth
    vmem = pltpu.MemorySpace.VMEM if hasattr(pltpu, "MemorySpace") else pltpu.VMEM
    return pl.pallas_call(
        coarse_kernel,
        out_shape=jax.ShapeDtypeStruct((depth, rows, cols), jnp.float32),
        in_specs=[
            pl.BlockSpec(memory_space=pltpu.SMEM),
            pl.BlockSpec(memory_space=vmem),
            pl.BlockSpec(memory_space=vmem),
            pl.BlockSpec(memory_space=vmem),
        ],
        out_specs=pl.BlockSpec(memory_space=vmem),
        scratch_shapes=[
            pltpu.VMEM((planes + 2, rows, cols), jnp.float32),
            pltpu.VMEM((planes + 2, rows, cols), jnp.float32),
        ],
        compiler_params=pltpu.CompilerParams(vmem_limit_bytes=48 * 1024 * 1024),
        cost_estimate=pl.CostEstimate(
            flops=2 * power * planes * rows * cols * 12,
            bytes_accessed=4 * planes * rows * cols * 3,
            transcendentals=0,
        ),
    )(jnp.stack([place, jnp.int32(power)]), slots, weight, scaled)


def per_device(forcing, conductivity, guess):
    stacked = jnp.concatenate([conductivity[None], forcing], axis=0)
    widened = extended(stacked, (("space", 1),), 1)
    kappa_wide = widened[0]
    fine_weight = step_length * kappa_wide
    fine_scaled = 1.0 + 6.0 * fine_weight

    n_sp = lax.axis_size("space")
    me_sp = lax.axis_index("space")
    order = lax.rem(me_sp - jnp.arange(n_sp, dtype=jnp.int32) + n_sp, n_sp)
    place = me_sp.astype(jnp.int32)

    def advance(state, weight, scaled, source):
        padded = extended(state, (("space", 0),), 2)
        target = padded[1:-1]
        if source is not None:
            target = target + step_length * source
        first = sweep_once(padded, target, weight, scaled)
        return sweep_once(first, target[1:-1], weight[1:-1], scaled[1:-1])

    def fine_step(state, index):
        return advance(state, fine_weight, fine_scaled, widened[1 + index])

    def relax(anchor):
        states = [anchor]
        for index in range(1, CF):
            states.append(fine_step(states[-1], index))
        return states

    anchor = guess[0]
    states = relax(anchor)
    before = shifted(states[-1], "tm", 1)
    defect = fine_step(before, 0) - anchor

    count = lax.axis_size("tm")
    depth = defect.shape[0]
    moved = shifted(defect, "tm", 1)
    slots = column_slabs(jnp.concatenate([moved, conductivity], axis=0), 0)
    kappa_full = jnp.take(slots[:, depth:], order, axis=0)
    kappa_full = kappa_full.reshape((-1,) + conductivity.shape[1:])
    coarse_weight = CF * step_length * kappa_full
    coarse_scaled = 1.0 + 6.0 * coarse_weight
    total = defect + coarse_power(1, place, slots[:, :depth], coarse_weight, coarse_scaled)
    lag = 2
    while lag < count:
        slots = column_slabs(total, lag)
        total = total + coarse_power(lag, place, slots, coarse_weight, coarse_scaled)
        lag *= 2
    anchor = anchor + total
    return jnp.stack(relax(anchor), axis=0)


def solution(mesh):
    in_specs = (P("tm", "space", None, None), P("space", None, None), P("tm", "space", None, None))
    out_specs = P("tm", "space", None, None)
    return jax.shard_map(
        per_device, mesh=mesh, in_specs=in_specs, out_specs=out_specs, check_vma=False
    )
```

```python
import functools

import jax
import jax.numpy as jnp
from jax import lax
from jax.experimental import pallas as pl
from jax.experimental.pallas import tpu as pltpu
from jax.sharding import PartitionSpec as P

CF = 4


step_length = 0.1


def extended(block, sides, width):
    for axis, dim in sides:
        count = lax.axis_size(axis)
        forward = [(i, i + 1) for i in range(count - 1)]
        backward = [(target, source) for source, target in forward]
        low = lax.ppermute(
            lax.slice_in_dim(block, block.shape[dim] - width, None, axis=dim), axis, forward
        )
        high = lax.ppermute(lax.slice_in_dim(block, 0, width, axis=dim), axis, backward)
        block = jnp.concatenate([low, block, high], axis=dim)
    return block


def shifted(value, axis, steps):
    count = lax.axis_size(axis)
    pairs = [(source, (source + steps) % count) for source in range(count)]
    return lax.ppermute(value, axis, pairs)


def neighbours(field):
    middle = field[1:-1]
    total = field[:-2] + field[2:]
    total = total + jnp.roll(middle, 1, axis=1) + jnp.roll(middle, -1, axis=1)
    return total + jnp.roll(middle, 1, axis=2) + jnp.roll(middle, -1, axis=2)


def sweep_once(field, target, weight, scaled):
    return (target + weight * neighbours(field)) / scaled


def column_slabs(slab, lag):
    if lag:
        slab = shifted(slab, "tm", lag)
    slots = [slab]
    for t in range(1, lax.axis_size("space")):
        slots.append(shifted(slab, "space", t))
    return jnp.stack(slots, axis=0)


def coarse_kernel(place_ref, slots_ref, w_ref, s_ref, o_ref, a_buf, b_buf):
    n_sp, depth, rows, cols = slots_ref.shape
    planes = n_sp * depth
    me = place_ref[0]
    power = place_ref[1]
    zero = jnp.zeros((rows, cols), jnp.float32)
    a_buf[0] = zero
    a_buf[planes + 1] = zero
    b_buf[0] = zero
    b_buf[planes + 1] = zero

    def load(q, carry):
        slot = lax.rem(me - q + n_sp, n_sp)
        for p in range(depth):
            a_buf[1 + q * depth + p] = slots_ref[slot, p]
        return carry

    lax.fori_loop(0, n_sp, load, 0)

    def sweep(src, dst, z):
        centre = src[z + 1]
        total = src[z] + src[z + 2]
        total = total + pltpu.roll(centre, 1, 0) + pltpu.roll(centre, rows - 1, 0)
        total = total + pltpu.roll(centre, 1, 1) + pltpu.roll(centre, cols - 1, 1)
        dst[z + 1] = (a_buf[z + 1] + w_ref[z] * total) / s_ref[z]

    def first(z, carry):
        sweep(a_buf, b_buf, z)
        return carry

    def second(z, carry):
        sweep(b_buf, a_buf, z)
        return carry

    def one(i, carry):
        lax.fori_loop(0, planes, first, 0, unroll=True)
        lax.fori_loop(0, planes, second, 0, unroll=True)
        return carry

    lax.fori_loop(0, power, one, 0)
    for p in range(depth):
        o_ref[p] = a_buf[1 + me * depth + p]


def coarse_power(power, place, slots, weight, scaled):
    n_sp, depth, rows, cols = slots.shape
    planes = n_sp * depth
    vmem = pltpu.MemorySpace.VMEM if hasattr(pltpu, "MemorySpace") else pltpu.VMEM
    return pl.pallas_call(
        coarse_kernel,
        out_shape=jax.ShapeDtypeStruct((depth, rows, cols), jnp.float32),
        in_specs=[
            pl.BlockSpec(memory_space=pltpu.SMEM),
            pl.BlockSpec(memory_space=vmem),
            pl.BlockSpec(memory_space=vmem),
            pl.BlockSpec(memory_space=vmem),
        ],
        out_specs=pl.BlockSpec(memory_space=vmem),
        scratch_shapes=[
            pltpu.VMEM((planes + 2, rows, cols), jnp.float32),
            pltpu.VMEM((planes + 2, rows, cols), jnp.float32),
        ],
        compiler_params=pltpu.CompilerParams(vmem_limit_bytes=48 * 1024 * 1024),
        cost_estimate=pl.CostEstimate(
            flops=2 * power * planes * rows * cols * 12,
            bytes_accessed=4 * planes * rows * cols * 3,
            transcendentals=0,
        ),
    )(jnp.stack([place, jnp.int32(power)]), slots, weight, scaled)


def per_device(forcing, conductivity, guess):
    stacked = jnp.concatenate([conductivity[None], forcing], axis=0)
    widened = extended(stacked, (("space", 1),), 1)
    kappa_wide = widened[0]
    fine_weight = step_length * kappa_wide
    fine_scaled = 1.0 + 6.0 * fine_weight

    n_sp = lax.axis_size("space")
    me_sp = lax.axis_index("space")
    order = lax.rem(me_sp - jnp.arange(n_sp, dtype=jnp.int32) + n_sp, n_sp)
    kappa_full = jnp.take(column_slabs(conductivity, 0), order, axis=0)
    kappa_full = kappa_full.reshape((-1,) + conductivity.shape[1:])
    coarse_weight = CF * step_length * kappa_full
    coarse_scaled = 1.0 + 6.0 * coarse_weight
    place = me_sp.astype(jnp.int32)

    def advance(state, weight, scaled, source):
        padded = extended(state, (("space", 0),), 2)
        target = padded[1:-1]
        if source is not None:
            target = target + step_length * source
        first = sweep_once(padded, target, weight, scaled)
        return sweep_once(first, target[1:-1], weight[1:-1], scaled[1:-1])

    def fine_step(state, index):
        return advance(state, fine_weight, fine_scaled, widened[1 + index])

    def relax(anchor):
        states = [anchor]
        for index in range(1, CF):
            states.append(fine_step(states[-1], index))
        return states

    anchor = guess[0]
    states = relax(anchor)
    before = shifted(states[-1], "tm", 1)
    defect = fine_step(before, 0) - anchor

    count = lax.axis_size("tm")
    depth = defect.shape[0]
    reach = 2 * min(2, count // 2)
    rim = jnp.zeros((reach,) + kappa_full.shape[1:], kappa_full.dtype)
    kappa_near = lax.dynamic_slice_in_dim(
        jnp.concatenate([rim, kappa_full, rim], axis=0), place * depth, depth + 2 * reach, axis=0
    )
    near_weight = CF * step_length * kappa_near
    near_scaled = 1.0 + 6.0 * near_weight

    def coarse_near(field, weight, scaled):
        first = (field[1:-1] + weight[1:-1] * neighbours(field)) / scaled[1:-1]
        return (field[2:-2] + weight[2:-2] * neighbours(first)) / scaled[2:-2]

    total = defect
    lag = 1
    while lag < count:
        moved = shifted(total, "tm", lag)
        if 2 * lag <= depth and lag <= 2:
            field = extended(moved, (("space", 0),), 2 * lag)
            for turn in range(lag):
                cut = reach - 2 * lag + 2 * turn
                field = coarse_near(
                    field, near_weight[cut: near_weight.shape[0] - cut],
                    near_scaled[cut: near_scaled.shape[0] - cut],
                )
            total = total + field
        else:
            slots = column_slabs(moved, 0)
            total = total + coarse_power(lag, place, slots, coarse_weight, coarse_scaled)
        lag *= 2
    anchor = anchor + total
    return jnp.stack(relax(anchor), axis=0)


def solution(mesh):
    in_specs = (P("tm", "space", None, None), P("space", None, None), P("tm", "space", None, None))
    out_specs = P("tm", "space", None, None)
    return jax.shard_map(
        per_device, mesh=mesh, in_specs=in_specs, out_specs=out_specs, check_vma=False
    )
```

```python
import functools

import jax
import jax.numpy as jnp
from jax import lax
from jax.experimental import pallas as pl
from jax.experimental.pallas import tpu as pltpu
from jax.sharding import PartitionSpec as P

CF = 4


step_length = 0.1


def extended(block, sides, width):
    for axis, dim in sides:
        count = lax.axis_size(axis)
        forward = [(i, i + 1) for i in range(count - 1)]
        backward = [(target, source) for source, target in forward]
        low = lax.ppermute(
            lax.slice_in_dim(block, block.shape[dim] - width, None, axis=dim), axis, forward
        )
        high = lax.ppermute(lax.slice_in_dim(block, 0, width, axis=dim), axis, backward)
        block = jnp.concatenate([low, block, high], axis=dim)
    return block


def shifted(value, axis, steps):
    count = lax.axis_size(axis)
    pairs = [(source, (source + steps) % count) for source in range(count)]
    return lax.ppermute(value, axis, pairs)


def neighbours(field):
    middle = field[1:-1]
    total = field[:-2] + field[2:]
    total = total + jnp.roll(middle, 1, axis=1) + jnp.roll(middle, -1, axis=1)
    return total + jnp.roll(middle, 1, axis=2) + jnp.roll(middle, -1, axis=2)


def sweep_once(field, target, weight, scaled):
    return (target + weight * neighbours(field)) / scaled


def near_halo(block, width):
    depth = block.shape[0]
    if width <= depth:
        return extended(block, (("space", 0),), width)
    count = lax.axis_size("space")
    lows, highs = [], []
    for distance in range(1, -(-width // depth) + 1):
        forward = [(i, i + distance) for i in range(count - distance)]
        backward = [(i + distance, i) for i in range(count - distance)]
        lows.insert(0, lax.ppermute(block, "space", forward))
        highs.append(lax.ppermute(block, "space", backward))
    field = jnp.concatenate(lows + [block] + highs, axis=0)
    extra = len(lows) * depth - width
    return field[extra: field.shape[0] - extra]


def column_slabs(slab, lag):
    if lag:
        slab = shifted(slab, "tm", lag)
    slots = [slab]
    for t in range(1, lax.axis_size("space")):
        slots.append(shifted(slab, "space", t))
    return jnp.stack(slots, axis=0)


def coarse_kernel(place_ref, slots_ref, w_ref, s_ref, o_ref, a_buf, b_buf):
    n_sp, depth, rows, cols = slots_ref.shape
    planes = n_sp * depth
    me = place_ref[0]
    power = place_ref[1]
    zero = jnp.zeros((rows, cols), jnp.float32)
    a_buf[0] = zero
    a_buf[planes + 1] = zero
    b_buf[0] = zero
    b_buf[planes + 1] = zero

    def load(q, carry):
        slot = lax.rem(me - q + n_sp, n_sp)
        for p in range(depth):
            a_buf[1 + q * depth + p] = slots_ref[slot, p]
        return carry

    lax.fori_loop(0, n_sp, load, 0)

    def sweep(src, dst, z):
        centre = src[z + 1]
        total = src[z] + src[z + 2]
        total = total + pltpu.roll(centre, 1, 0) + pltpu.roll(centre, rows - 1, 0)
        total = total + pltpu.roll(centre, 1, 1) + pltpu.roll(centre, cols - 1, 1)
        dst[z + 1] = (a_buf[z + 1] + w_ref[z] * total) / s_ref[z]

    def first(z, carry):
        sweep(a_buf, b_buf, z)
        return carry

    def second(z, carry):
        sweep(b_buf, a_buf, z)
        return carry

    def one(i, carry):
        lax.fori_loop(0, planes, first, 0, unroll=True)
        lax.fori_loop(0, planes, second, 0, unroll=True)
        return carry

    lax.fori_loop(0, power, one, 0)
    for p in range(depth):
        o_ref[p] = a_buf[1 + me * depth + p]


def coarse_power(power, place, slots, weight, scaled):
    n_sp, depth, rows, cols = slots.shape
    planes = n_sp * depth
    vmem = pltpu.MemorySpace.VMEM if hasattr(pltpu, "MemorySpace") else pltpu.VMEM
    return pl.pallas_call(
        coarse_kernel,
        out_shape=jax.ShapeDtypeStruct((depth, rows, cols), jnp.float32),
        in_specs=[
            pl.BlockSpec(memory_space=pltpu.SMEM),
            pl.BlockSpec(memory_space=vmem),
            pl.BlockSpec(memory_space=vmem),
            pl.BlockSpec(memory_space=vmem),
        ],
        out_specs=pl.BlockSpec(memory_space=vmem),
        scratch_shapes=[
            pltpu.VMEM((planes + 2, rows, cols), jnp.float32),
            pltpu.VMEM((planes + 2, rows, cols), jnp.float32),
        ],
        compiler_params=pltpu.CompilerParams(vmem_limit_bytes=48 * 1024 * 1024),
        cost_estimate=pl.CostEstimate(
            flops=2 * power * planes * rows * cols * 12,
            bytes_accessed=4 * planes * rows * cols * 3,
            transcendentals=0,
        ),
    )(jnp.stack([place, jnp.int32(power)]), slots, weight, scaled)


def per_device(forcing, conductivity, guess):
    stacked = jnp.concatenate([conductivity[None], forcing], axis=0)
    widened = extended(stacked, (("space", 1),), 1)
    kappa_wide = widened[0]
    fine_weight = step_length * kappa_wide
    fine_scaled = 1.0 + 6.0 * fine_weight

    n_sp = lax.axis_size("space")
    me_sp = lax.axis_index("space")
    order = lax.rem(me_sp - jnp.arange(n_sp, dtype=jnp.int32) + n_sp, n_sp)
    kappa_full = jnp.take(column_slabs(conductivity, 0), order, axis=0)
    kappa_full = kappa_full.reshape((-1,) + conductivity.shape[1:])
    coarse_weight = CF * step_length * kappa_full
    coarse_scaled = 1.0 + 6.0 * coarse_weight
    place = me_sp.astype(jnp.int32)

    def advance(state, weight, scaled, source):
        padded = extended(state, (("space", 0),), 2)
        target = padded[1:-1]
        if source is not None:
            target = target + step_length * source
        first = sweep_once(padded, target, weight, scaled)
        return sweep_once(first, target[1:-1], weight[1:-1], scaled[1:-1])

    def fine_step(state, index):
        return advance(state, fine_weight, fine_scaled, widened[1 + index])

    def relax(anchor):
        states = [anchor]
        for index in range(1, CF):
            states.append(fine_step(states[-1], index))
        return states

    anchor = guess[0]
    states = relax(anchor)
    before = shifted(states[-1], "tm", 1)
    defect = fine_step(before, 0) - anchor

    count = lax.axis_size("tm")
    depth = defect.shape[0]
    reach = 2 * min(depth, count // 2)
    rim = jnp.zeros((reach,) + kappa_full.shape[1:], kappa_full.dtype)
    kappa_near = lax.dynamic_slice_in_dim(
        jnp.concatenate([rim, kappa_full, rim], axis=0), place * depth, depth + 2 * reach, axis=0
    )
    near_weight = CF * step_length * kappa_near
    near_scaled = 1.0 + 6.0 * near_weight

    def coarse_near(field, weight, scaled):
        first = (field[1:-1] + weight[1:-1] * neighbours(field)) / scaled[1:-1]
        return (field[2:-2] + weight[2:-2] * neighbours(first)) / scaled[2:-2]

    total = defect
    lag = 1
    while lag < count:
        moved = shifted(total, "tm", lag)
        if 2 * lag <= reach:
            field = near_halo(moved, 2 * lag)
            for turn in range(lag):
                cut = reach - 2 * lag + 2 * turn
                field = coarse_near(
                    field, near_weight[cut: near_weight.shape[0] - cut],
                    near_scaled[cut: near_scaled.shape[0] - cut],
                )
            total = total + field
        else:
            slots = column_slabs(moved, 0)
            total = total + coarse_power(lag, place, slots, coarse_weight, coarse_scaled)
        lag *= 2
    anchor = anchor + total
    return jnp.stack(relax(anchor), axis=0)


def solution(mesh):
    in_specs = (P("tm", "space", None, None), P("space", None, None), P("tm", "space", None, None))
    out_specs = P("tm", "space", None, None)
    return jax.shard_map(
        per_device, mesh=mesh, in_specs=in_specs, out_specs=out_specs, check_vma=False
    )
```

```python
import functools

import jax
import jax.numpy as jnp
from jax import lax
from jax.experimental import pallas as pl
from jax.experimental.pallas import tpu as pltpu
from jax.sharding import PartitionSpec as P

CF = 4


step_length = 0.1


def extended(block, sides, width):
    for axis, dim in sides:
        count = lax.axis_size(axis)
        forward = [(i, i + 1) for i in range(count - 1)]
        backward = [(target, source) for source, target in forward]
        low = lax.ppermute(
            lax.slice_in_dim(block, block.shape[dim] - width, None, axis=dim), axis, forward
        )
        high = lax.ppermute(lax.slice_in_dim(block, 0, width, axis=dim), axis, backward)
        block = jnp.concatenate([low, block, high], axis=dim)
    return block


def shifted(value, axis, steps):
    count = lax.axis_size(axis)
    pairs = [(source, (source + steps) % count) for source in range(count)]
    return lax.ppermute(value, axis, pairs)


def neighbours(field):
    middle = field[1:-1]
    total = field[:-2] + field[2:]
    total = total + jnp.roll(middle, 1, axis=1) + jnp.roll(middle, -1, axis=1)
    return total + jnp.roll(middle, 1, axis=2) + jnp.roll(middle, -1, axis=2)


def sweep_once(field, target, weight, scaled):
    return (target + weight * neighbours(field)) / scaled


def near_halo(block, width):
    depth = block.shape[0]
    if width <= depth:
        return extended(block, (("space", 0),), width)
    count = lax.axis_size("space")
    lows, highs = [], []
    for distance in range(1, -(-width // depth) + 1):
        forward = [(i, i + distance) for i in range(count - distance)]
        backward = [(i + distance, i) for i in range(count - distance)]
        lows.insert(0, lax.ppermute(block, "space", forward))
        highs.append(lax.ppermute(block, "space", backward))
    field = jnp.concatenate(lows + [block] + highs, axis=0)
    extra = len(lows) * depth - width
    return field[extra: field.shape[0] - extra]


def column_slabs(slab, lag):
    if lag:
        slab = shifted(slab, "tm", lag)
    slots = [slab]
    for t in range(1, lax.axis_size("space")):
        slots.append(shifted(slab, "space", t))
    return jnp.stack(slots, axis=0)


def coarse_kernel(place_ref, slots_ref, w_ref, s_ref, o_ref, a_buf, b_buf):
    n_sp, depth, rows, cols = slots_ref.shape
    planes = n_sp * depth
    me = place_ref[0]
    power = place_ref[1]
    zero = jnp.zeros((rows, cols), jnp.float32)
    a_buf[0] = zero
    a_buf[planes + 1] = zero
    b_buf[0] = zero
    b_buf[planes + 1] = zero

    def load(q, carry):
        slot = lax.rem(me - q + n_sp, n_sp)
        for p in range(depth):
            a_buf[1 + q * depth + p] = slots_ref[slot, p]
        return carry

    lax.fori_loop(0, n_sp, load, 0)

    def sweep(src, dst, z):
        centre = src[z + 1]
        total = src[z] + src[z + 2]
        total = total + pltpu.roll(centre, 1, 0) + pltpu.roll(centre, rows - 1, 0)
        total = total + pltpu.roll(centre, 1, 1) + pltpu.roll(centre, cols - 1, 1)
        dst[z + 1] = (a_buf[z + 1] + w_ref[z] * total) / s_ref[z]

    def first(z, carry):
        sweep(a_buf, b_buf, z)
        return carry

    def second(z, carry):
        sweep(b_buf, a_buf, z)
        return carry

    def one(i, carry):
        lax.fori_loop(0, planes, first, 0, unroll=True)
        lax.fori_loop(0, planes, second, 0, unroll=True)
        return carry

    lax.fori_loop(0, power, one, 0)
    for p in range(depth):
        o_ref[p] = a_buf[1 + me * depth + p]


def coarse_power(power, place, slots, weight, scaled):
    n_sp, depth, rows, cols = slots.shape
    planes = n_sp * depth
    vmem = pltpu.MemorySpace.VMEM if hasattr(pltpu, "MemorySpace") else pltpu.VMEM
    return pl.pallas_call(
        coarse_kernel,
        out_shape=jax.ShapeDtypeStruct((depth, rows, cols), jnp.float32),
        in_specs=[
            pl.BlockSpec(memory_space=pltpu.SMEM),
            pl.BlockSpec(memory_space=vmem),
            pl.BlockSpec(memory_space=vmem),
            pl.BlockSpec(memory_space=vmem),
        ],
        out_specs=pl.BlockSpec(memory_space=vmem),
        scratch_shapes=[
            pltpu.VMEM((planes + 2, rows, cols), jnp.float32),
            pltpu.VMEM((planes + 2, rows, cols), jnp.float32),
        ],
        compiler_params=pltpu.CompilerParams(vmem_limit_bytes=48 * 1024 * 1024),
        cost_estimate=pl.CostEstimate(
            flops=2 * power * planes * rows * cols * 12,
            bytes_accessed=4 * planes * rows * cols * 3,
            transcendentals=0,
        ),
    )(jnp.stack([place, jnp.int32(power)]), slots, weight, scaled)


def per_device(forcing, conductivity, guess):
    stacked = jnp.concatenate([conductivity[None], forcing, guess], axis=0)
    halo = extended(stacked, (("space", 1),), 2)
    widened = halo[:-1, 1:-1]
    padded_guess = halo[-1]
    kappa_wide = widened[0]
    fine_weight = step_length * kappa_wide
    fine_scaled = 1.0 + 6.0 * fine_weight

    n_sp = lax.axis_size("space")
    me_sp = lax.axis_index("space")
    order = lax.rem(me_sp - jnp.arange(n_sp, dtype=jnp.int32) + n_sp, n_sp)
    kappa_full = jnp.take(column_slabs(conductivity, 0), order, axis=0)
    kappa_full = kappa_full.reshape((-1,) + conductivity.shape[1:])
    coarse_weight = CF * step_length * kappa_full
    coarse_scaled = 1.0 + 6.0 * coarse_weight
    place = me_sp.astype(jnp.int32)

    def advance(state, weight, scaled, source, padded=None):
        if padded is None:
            padded = extended(state, (("space", 0),), 2)
        target = padded[1:-1]
        if source is not None:
            target = target + step_length * source
        first = sweep_once(padded, target, weight, scaled)
        return sweep_once(first, target[1:-1], weight[1:-1], scaled[1:-1])

    def fine_step(state, index, padded=None):
        return advance(state, fine_weight, fine_scaled, widened[1 + index], padded)

    def relax(anchor, padded=None):
        states = [anchor]
        for index in range(1, CF):
            states.append(fine_step(states[-1], index, padded if index == 1 else None))
        return states

    anchor = guess[0]
    states = relax(anchor, padded_guess)
    before = shifted(states[-1], "tm", 1)
    defect = fine_step(before, 0) - anchor

    count = lax.axis_size("tm")
    depth = defect.shape[0]
    reach = 2 * min(depth, count // 2)
    rim = jnp.zeros((reach,) + kappa_full.shape[1:], kappa_full.dtype)
    kappa_near = lax.dynamic_slice_in_dim(
        jnp.concatenate([rim, kappa_full, rim], axis=0), place * depth, depth + 2 * reach, axis=0
    )
    near_weight = CF * step_length * kappa_near
    near_scaled = 1.0 + 6.0 * near_weight

    def coarse_near(field, weight, scaled):
        first = (field[1:-1] + weight[1:-1] * neighbours(field)) / scaled[1:-1]
        return (field[2:-2] + weight[2:-2] * neighbours(first)) / scaled[2:-2]

    total = defect
    lag = 1
    while lag < count:
        moved = shifted(total, "tm", lag)
        if 2 * lag <= reach:
            field = near_halo(moved, 2 * lag)
            for turn in range(lag):
                cut = reach - 2 * lag + 2 * turn
                field = coarse_near(
                    field, near_weight[cut: near_weight.shape[0] - cut],
                    near_scaled[cut: near_scaled.shape[0] - cut],
                )
            total = total + field
        else:
            slots = column_slabs(moved, 0)
            total = total + coarse_power(lag, place, slots, coarse_weight, coarse_scaled)
        lag *= 2
    anchor = anchor + total
    return jnp.stack(relax(anchor), axis=0)


def solution(mesh):
    in_specs = (P("tm", "space", None, None), P("space", None, None), P("tm", "space", None, None))
    out_specs = P("tm", "space", None, None)
    return jax.shard_map(
        per_device, mesh=mesh, in_specs=in_specs, out_specs=out_specs, check_vma=False
    )
```
